256 devices in a mesh: section: 8 (over x, z_lo), expert: 32 (over z_hi, y, core).
Axes of the slice: x: 4, y: 4, z: 8 (z_hi: 4, z_lo: 2; z = z_hi * 2 + z_lo), core: 2. Of those that a mesh axis runs over, the one named last changes fastest.
Arguments:
- grad_out: bfloat16 [8, 6144, 2048], P('section', 'expert'), may hold values from -6 to 6
- layer_input: bfloat16 [8, 6144, 2048], P('section', 'expert'), may hold values from -6 to 6
- routes: int32 [8, 6144, 8], P('section', 'expert'), may hold values from 0 to 127, as said below
- route_logits: float32 [8, 6144, 8], P('section', 'expert'), may hold values from -6 to 6
- gate_weight: bfloat16 [8, 32, 2048, 768], P('section', 'expert'), may hold values from -0.125 to 0.125
- up_weight: bfloat16 [8, 32, 2048, 768], P('section', 'expert'), may hold values from -0.125 to 0.125
- down_weight: bfloat16 [8, 32, 768, 2048], P('section', 'expert'), may hold values from -0.21875 to 0.21875
- router_weight: bfloat16 [8, 2048, 128], P('section'), may hold values from -0.125 to 0.125
Outputs:
- grad_in: bfloat16 [8, 6144, 2048], P('section', 'expert')
- route_logit_grad: float32 [8, 6144, 8], P('section', 'expert')
The draws below stay inside these ranges and needn't reach their ends.
Inputs may be any that keep to these rules, and one draw needn't show every extreme that they name: `routes`: each token names 8 different experts. Among the tokens of one device no expert is named more than 24 times, and in every section one expert below 32 is named exactly 24 times by the tokens of every device of that section.
All inputs are finite; a program needn't handle non-finite values.
Results may differ from the reference program's by a relative error of at most 0.004.
Values may be sent and summed in bfloat16 or wider, within the bound.
No kernel may reach another device: no remote copies, remote signals or barrier semaphores. Data moves between devices by JAX's collectives and lax.ppermute only.
A program may use at most 128 MiB of HBM per device.

```python
import jax
import jax.numpy as jnp
from jax import lax

D = 2048
FF = 768
TOP = 8
T_DEV = 192
TOKENS = 6144
EXPERTS = 32
EXP_ALL = 128
CAP = 24
N_SECTION = 8
N_EXPERT = 32


def routes_block(key, hottest):
    mean_load = T_DEV * TOP // EXP_ALL
    subkeys = jax.random.split(key, 4)
    ranking = jax.random.permutation(subkeys[0], EXP_ALL).astype(jnp.int32)
    where_hot = jnp.argmax(ranking == hottest)
    ranking = ranking.at[where_hot].set(ranking[0]).at[0].set(hottest)
    offsets = jax.random.randint(subkeys[1], (EXP_ALL // 2,), 0, mean_load + 1).astype(jnp.int32)
    offsets = offsets.at[0].set(mean_load)
    loads = jnp.stack([mean_load + offsets, mean_load - offsets], axis=1).reshape(EXP_ALL)
    boundaries = jnp.cumsum(loads).astype(jnp.int32)
    positions = jnp.arange(T_DEV * TOP, dtype=jnp.int32)
    rank_of = jnp.sum((boundaries[None, :] <= positions[:, None]).astype(jnp.int32), axis=1)
    assigned = ranking[rank_of].reshape(TOP, T_DEV).T
    row_order = jax.random.permutation(subkeys[2], T_DEV)
    assigned = assigned[row_order]
    scores = jax.random.randint(subkeys[3], (T_DEV, TOP), 0, 1 << 20).astype(jnp.int32) * TOP + jnp.arange(TOP, dtype=jnp.int32)[None, :]
    assigned = jnp.take_along_axis(assigned, jnp.argsort(scores, axis=1), axis=1)
    return assigned.astype(jnp.int32)


def draw_routes(key, part):
    hottest = jax.random.randint(jax.random.fold_in(key, 7), (N_SECTION,), 0, EXPERTS).astype(jnp.int32)
    block_keys = jax.random.split(jax.random.fold_in(key, 11), N_SECTION * N_EXPERT)
    section_hot = jnp.repeat(hottest, N_EXPERT)
    blocks = jax.vmap(routes_block)(block_keys, section_hot)
    return blocks.reshape(N_SECTION, N_EXPERT * T_DEV, TOP)


def block_levels(rng, extent, pieces, low, top_value):
    loudness = 1.0
    for axis_at, blocks in pieces:
        heights = jax.random.uniform(jax.random.fold_in(jax.random.fold_in(rng, 6), axis_at), (blocks,), jnp.float32, low / len(pieces), top_value / len(pieces))
        loudness = loudness * jnp.repeat(jnp.exp(heights), extent[axis_at] // blocks).reshape((-1,) + (1,) * (len(extent) - 1 - axis_at))
    return loudness


def gaussian(rng, extent, scale, bound, cuts=(), kind=jnp.bfloat16):
    values = scale * jax.random.normal(rng, extent, jnp.float32)
    if cuts:
        values = values * block_levels(rng, extent, cuts, -0.22, 0.18)
    return jnp.clip(values, -bound, bound).astype(kind)


def setup_inputs(seed: int = 0) -> dict:
    seeds = jax.random.split(jax.random.key(seed), 9)
    grad_out = gaussian(seeds[0], (N_SECTION, TOKENS, D), 1.0, 6.0, ((0, 8), (1, 32)))
    layer_input = gaussian(seeds[1], (N_SECTION, TOKENS, D), 1.0, 6.0, ((0, 8), (1, 32)))
    routes = draw_routes(jax.random.fold_in(seeds[8], 71), 0)
    route_logits = gaussian(seeds[3], (N_SECTION, TOKENS, TOP), 1.5, 6.0, ((0, 8), (1, 32)), jnp.float32)
    gate_weight = gaussian(seeds[4], (N_SECTION, EXPERTS, D, FF), D ** -0.5, 0.125, ((0, 8), (1, 32)))
    up_weight = gaussian(seeds[5], (N_SECTION, EXPERTS, D, FF), D ** -0.5, 0.125, ((0, 8), (1, 32)))
    down_weight = gaussian(seeds[6], (N_SECTION, EXPERTS, FF, D), FF ** -0.5, 0.21875, ((0, 8), (1, 32)))
    router_weight = gaussian(seeds[7], (N_SECTION, D, EXP_ALL), D ** -0.5, 0.125, ((0, 8),))
    return dict(grad_out=grad_out, layer_input=layer_input, routes=routes, route_logits=route_logits, gate_weight=gate_weight, up_weight=up_weight, down_weight=down_weight, router_weight=router_weight)


def expert_rows(inputs, grad_rows, w_gate, w_up, w_down):
    pre_gate = jnp.dot(inputs, w_gate, preferred_element_type=jnp.float32)
    pre_up = jnp.dot(inputs, w_up, preferred_element_type=jnp.float32)
    hidden_grad = jnp.dot(grad_rows, w_down.T, preferred_element_type=jnp.float32)
    sigmoid_gate = jax.nn.sigmoid(pre_gate)
    activation = pre_gate * sigmoid_gate
    weight_grad = jnp.sum(hidden_grad * activation * pre_up, axis=-1).astype(jnp.bfloat16)
    gate_grad = (hidden_grad * pre_up * sigmoid_gate * (1.0 + pre_gate * (1.0 - sigmoid_gate))).astype(jnp.bfloat16)
    up_grad = (hidden_grad * activation).astype(jnp.bfloat16)
    pair_grad = jnp.dot(gate_grad, w_gate.T, preferred_element_type=jnp.float32) + jnp.dot(up_grad, w_up.T, preferred_element_type=jnp.float32)
    return pair_grad.astype(jnp.bfloat16), weight_grad


def section_back(operands):
    incoming, inputs, picks, logits, w_gates, w_ups, w_downs, w_router = operands
    token_count = inputs.shape[0]
    top_count = picks.shape[1]
    flat_routes = picks.reshape(-1).astype(jnp.int32)
    route_count = flat_routes.shape[0]
    exponent = jnp.exp(logits)
    route_weight = exponent / jnp.sum(exponent, axis=1, keepdims=True)
    onehot = (flat_routes[:, None] == jnp.arange(EXPERTS, dtype=jnp.int32)[None, :]).astype(jnp.int32)
    rank_inside = jnp.sum((jnp.cumsum(onehot, axis=0) - 1) * onehot, axis=1).astype(jnp.int32)
    width_all = N_EXPERT * CAP
    slot_index = jnp.where(flat_routes < EXPERTS, flat_routes * width_all + rank_inside, EXPERTS * width_all).astype(jnp.int32)
    slot_owner = jnp.full((EXPERTS * width_all + 1,), route_count, jnp.int32)
    slot_owner = slot_owner.at[slot_index].set(jnp.arange(route_count, dtype=jnp.int32))
    slot_owner = slot_owner[: EXPERTS * width_all].reshape(EXPERTS, width_all)
    padded_in = jnp.concatenate([inputs, jnp.zeros((1, D), inputs.dtype)], axis=0)
    padded_grad = jnp.concatenate([incoming, jnp.zeros((1, D), incoming.dtype)], axis=0)
    flat_weight = jnp.concatenate([route_weight.reshape(-1), jnp.zeros((1,), jnp.float32)], axis=0)

    def per_expert(carry, operand):
        expert_sum, weight_flat = carry
        row_ids, w_gate, w_up, w_down = operand
        token_index = jnp.where(row_ids < route_count, row_ids // top_count, token_count).astype(jnp.int32)
        pair_grad, weight_grad = expert_rows(padded_in[token_index], padded_grad[token_index], w_gate, w_up, w_down)
        pair_weight = flat_weight[row_ids]
        expert_sum = expert_sum.at[token_index].add(pair_weight[:, None] * pair_grad.astype(jnp.float32))
        weight_flat = weight_flat.at[row_ids].add(weight_grad.astype(jnp.float32))
        return (expert_sum, weight_flat), None

    initial = (jnp.zeros((token_count + 1, D), jnp.float32), jnp.zeros((route_count + 1,), jnp.float32))
    (expert_sum, weight_flat), unused = lax.scan(per_expert, initial, (slot_owner, w_gates, w_ups, w_downs))
    weight_grad = weight_flat[:route_count].reshape(token_count, top_count)
    center = jnp.sum(route_weight * weight_grad, axis=1, keepdims=True)
    logit_grad = route_weight * (weight_grad - center)
    dense_grad = jnp.zeros((token_count, EXP_ALL), jnp.float32)
    dense_grad = dense_grad.at[jnp.arange(token_count, dtype=jnp.int32)[:, None], picks.astype(jnp.int32)].add(logit_grad)
    router_grad = jnp.dot(dense_grad, w_router.astype(jnp.float32).T, precision=lax.Precision.HIGHEST)
    grad_in = (incoming.astype(jnp.float32) + expert_sum[:token_count] + router_grad).astype(jnp.bfloat16)
    return grad_in, logit_grad


def reference(grad_out, layer_input, routes, route_logits, gate_weight, up_weight, down_weight, router_weight):
    incoming = jnp.roll(grad_out, -1, axis=0)
    grad_in, logit_grad = lax.map(section_back, (incoming, layer_input, routes, route_logits, gate_weight, up_weight, down_weight, router_weight))
    return grad_in, logit_grad
```

```python
import jax
import jax.numpy as jnp
from jax import lax
from jax.sharding import PartitionSpec as P


def from_behind(shard, axis, by):
    size = lax.axis_size(axis)
    return lax.ppermute(shard, axis, [(i, (i + by) % size) for i in range(size)])


def expert_rows(inputs, grad_rows, w_gate, w_up, w_down):
    pre_gate = jnp.dot(inputs, w_gate, preferred_element_type=jnp.float32)
    pre_up = jnp.dot(inputs, w_up, preferred_element_type=jnp.float32)
    hidden_grad = jnp.dot(grad_rows, w_down.T, preferred_element_type=jnp.float32)
    sigmoid_gate = jax.nn.sigmoid(pre_gate)
    activation = pre_gate * sigmoid_gate
    weight_grad = jnp.sum(hidden_grad * activation * pre_up, axis=-1).astype(jnp.bfloat16)
    gate_grad = (
        hidden_grad * pre_up * sigmoid_gate * (1.0 + pre_gate * (1.0 - sigmoid_gate))
    ).astype(jnp.bfloat16)
    up_grad = (hidden_grad * activation).astype(jnp.bfloat16)
    pair_grad = jnp.dot(gate_grad, w_gate.T, preferred_element_type=jnp.float32) + jnp.dot(
        up_grad, w_up.T, preferred_element_type=jnp.float32
    )
    return (pair_grad.astype(jnp.bfloat16), weight_grad)


def split_bf16(values, parts):
    pieces = []
    rest = values
    for _ in range(parts):
        piece = rest.astype(jnp.bfloat16)
        pieces.append(piece)
        rest = rest - piece.astype(jnp.float32)
    return pieces


def per_device(
    grad_out, layer_input, routes, route_logits, gate_weight, up_weight, down_weight, router_weight
):
    incoming = from_behind(grad_out, "section", -1)[0]
    x_in = layer_input[0]
    token_count, width_model = x_in.shape
    top_count = routes.shape[2]
    expert_count = lax.axis_size("expert")
    every_expert = router_weight.shape[2]
    capacity = 2 * token_count * top_count // every_expert
    slots_all = expert_count * capacity
    chunks = 2 if capacity % 2 == 0 else 1
    per_chunk = capacity // chunks
    w_gate = gate_weight[0, 0]
    w_up = up_weight[0, 0]
    w_down = down_weight[0, 0]
    w_router = router_weight[0]
    picks = routes[0]

    experts = jnp.arange(expert_count, dtype=jnp.int32)
    hit = picks[:, :, None] == experts[None, None, :]
    per_token = jnp.sum(hit.astype(jnp.float32), axis=1).astype(jnp.bfloat16)
    token_ids = jnp.arange(token_count, dtype=jnp.int32)
    before = (token_ids[None, :] < token_ids[:, None]).astype(jnp.bfloat16)
    earlier = jnp.dot(before, per_token, preferred_element_type=jnp.float32).astype(jnp.int32)
    rank_inside = jnp.sum(jnp.where(hit, earlier[:, None, :], 0), axis=2)
    slot_index = jnp.where(picks < expert_count, picks * capacity + rank_inside, slots_all)

    exponent = jnp.exp(route_logits[0])
    route_weight = exponent / jnp.sum(exponent, axis=1, keepdims=True)

    slot_ids = jnp.arange(slots_all, dtype=jnp.int32)
    slot_by_pick = slot_index.T
    weight_by_pick = route_weight.T
    pack = jnp.zeros((slots_all, token_count), jnp.float32)
    combine = jnp.zeros((token_count, slots_all), jnp.float32)
    for k in range(top_count):
        pack = pack + (slot_ids[:, None] == slot_by_pick[k][None, :]).astype(jnp.float32)
        combine = combine + jnp.where(
            slot_by_pick[k][:, None] == slot_ids[None, :], weight_by_pick[k][:, None], 0.0
        )
    pack = pack.astype(jnp.bfloat16).reshape(expert_count, capacity, token_count)
    combine = combine.reshape(token_count, expert_count, capacity)
    both_rows = jnp.concatenate([x_in, incoming], axis=1)

    expert_sum = jnp.zeros((token_count, width_model), jnp.float32)
    dots = []
    for c in range(chunks):
        lo = c * per_chunk
        pack_c = pack[:, lo : lo + per_chunk].reshape(-1, token_count)
        sent = jnp.dot(pack_c, both_rows, preferred_element_type=jnp.float32).astype(jnp.bfloat16)
        sent = sent.reshape(expert_count, per_chunk, 2 * width_model)
        got = lax.all_to_all(sent, "expert", split_axis=0, concat_axis=0, tiled=True)
        got = got.reshape(-1, 2 * width_model)
        pair_grad, weight_grad = expert_rows(
            got[:, :width_model], got[:, width_model:], w_gate, w_up, w_down
        )
        back_rows = lax.all_to_all(
            pair_grad.reshape(expert_count, per_chunk, width_model),
            "expert", split_axis=0, concat_axis=0, tiled=True,
        ).reshape(-1, width_model)
        back_dots = lax.all_to_all(
            weight_grad.reshape(expert_count, per_chunk),
            "expert", split_axis=0, concat_axis=0, tiled=True,
        )
        dots.append(back_dots)
        combine_c = combine[:, :, lo : lo + per_chunk].reshape(token_count, -1)
        for part in split_bf16(combine_c, 2):
            expert_sum = expert_sum + jnp.dot(part, back_rows, preferred_element_type=jnp.float32)

    slot_dots = jnp.concatenate(dots, axis=1).reshape(slots_all).astype(jnp.float32)
    weight_grad = jnp.sum(
        jnp.where(slot_index[:, :, None] == slot_ids[None, None, :], slot_dots[None, None, :], 0.0),
        axis=2,
    )
    center = jnp.sum(route_weight * weight_grad, axis=1, keepdims=True)
    logit_grad = route_weight * (weight_grad - center)
    matches = picks[:, :, None] == jnp.arange(every_expert, dtype=jnp.int32)[None, None, :]
    dense_grad = jnp.sum(jnp.where(matches, logit_grad[:, :, None], 0.0), axis=1)
    router_grad = jnp.zeros((token_count, width_model), jnp.float32)
    for part in split_bf16(dense_grad, 3):
        router_grad = router_grad + lax.dot_general(
            part, w_router, (((1,), (1,)), ((), ())), preferred_element_type=jnp.float32
        )
    grad_in = (incoming.astype(jnp.float32) + expert_sum + router_grad).astype(jnp.bfloat16)
    return (grad_in[None], logit_grad[None])


def solution(mesh):
    in_specs = (
        P("section", "expert", None),
        P("section", "expert", None),
        P("section", "expert", None),
        P("section", "expert", None),
        P("section", "expert", None, None),
        P("section", "expert", None, None),
        P("section", "expert", None, None),
        P("section", None, None),
    )
    out_specs = (P("section", "expert", None), P("section", "expert", None))
    return jax.shard_map(
        per_device, mesh=mesh, in_specs=in_specs, out_specs=out_specs, check_vma=False
    )
```

```python
import jax
import jax.numpy as jnp
from jax import lax
from jax.sharding import PartitionSpec as P


def from_behind(shard, axis, by):
    size = lax.axis_size(axis)
    return lax.ppermute(shard, axis, [(i, (i + by) % size) for i in range(size)])


def split_bf16(values, parts):
    pieces = []
    rest = values
    for _ in range(parts):
        piece = rest.astype(jnp.bfloat16)
        pieces.append(piece)
        rest = rest - piece.astype(jnp.float32)
    return pieces


def per_device(
    grad_out, layer_input, routes, route_logits, gate_weight, up_weight, down_weight, router_weight
):
    incoming = from_behind(grad_out, "section", -1)[0]
    x_in = layer_input[0]
    token_count, width_model = x_in.shape
    top_count = routes.shape[2]
    expert_count = lax.axis_size("expert")
    every_expert = router_weight.shape[2]
    capacity = 2 * token_count * top_count // every_expert
    slots_all = expert_count * capacity
    w_gate = gate_weight[0, 0]
    w_up = up_weight[0, 0]
    w_down = down_weight[0, 0]
    w_router = router_weight[0]
    picks = routes[0]

    experts = jnp.arange(expert_count, dtype=jnp.int32)
    hit = picks[:, :, None] == experts[None, None, :]
    per_token = jnp.sum(hit.astype(jnp.float32), axis=1).astype(jnp.bfloat16)
    token_ids = jnp.arange(token_count, dtype=jnp.int32)
    before = (token_ids[None, :] < token_ids[:, None]).astype(jnp.bfloat16)
    earlier = jnp.dot(before, per_token, preferred_element_type=jnp.float32).astype(jnp.int32)
    rank_inside = jnp.sum(jnp.where(hit, earlier[:, None, :], 0), axis=2)
    slot_index = jnp.where(picks < expert_count, picks * capacity + rank_inside, slots_all)

    exponent = jnp.exp(route_logits[0])
    route_weight = exponent / jnp.sum(exponent, axis=1, keepdims=True)

    slot_ids = jnp.arange(slots_all, dtype=jnp.int32).reshape(expert_count, capacity)
    pack = jnp.zeros((expert_count, capacity, token_count), jnp.float32)
    combine = jnp.zeros((token_count, expert_count, capacity), jnp.float32)
    for k in range(top_count):
        chosen = slot_index[:, k]
        pack = pack + (slot_ids[:, :, None] == chosen[None, None, :]).astype(jnp.float32)
        combine = combine + jnp.where(
            chosen[:, None, None] == slot_ids[None, :, :], route_weight[:, k][:, None, None], 0.0
        )
    pack = pack.astype(jnp.bfloat16)

    def pack_rows(rows):
        sent = jnp.einsum("est,td->esd", pack, rows, preferred_element_type=jnp.float32)
        return sent.astype(jnp.bfloat16)

    def exchange(block):
        return lax.all_to_all(block, "expert", split_axis=0, concat_axis=0, tiled=True)

    inputs = exchange(pack_rows(x_in))
    grad_rows = exchange(pack_rows(incoming))
    pre_gate = jnp.einsum("esd,df->esf", inputs, w_gate, preferred_element_type=jnp.float32)
    pre_up = jnp.einsum("esd,df->esf", inputs, w_up, preferred_element_type=jnp.float32)
    hidden_grad = jnp.einsum("esd,fd->esf", grad_rows, w_down, preferred_element_type=jnp.float32)
    sigmoid_gate = jax.nn.sigmoid(pre_gate)
    activation = pre_gate * sigmoid_gate
    pair_dots = jnp.sum(hidden_grad * activation * pre_up, axis=-1).astype(jnp.bfloat16)
    gate_grad = (
        hidden_grad * pre_up * sigmoid_gate * (1.0 + pre_gate * (1.0 - sigmoid_gate))
    ).astype(jnp.bfloat16)
    up_grad = (hidden_grad * activation).astype(jnp.bfloat16)
    returned_dots = exchange(pair_dots)
    pair_rows = jnp.einsum(
        "esf,df->esd", gate_grad, w_gate, preferred_element_type=jnp.float32
    ) + jnp.einsum("esf,df->esd", up_grad, w_up, preferred_element_type=jnp.float32)
    returned_rows = exchange(pair_rows.astype(jnp.bfloat16))

    slot_dots = returned_dots.astype(jnp.float32)
    weight_grad = jnp.sum(
        jnp.where(
            slot_index[:, :, None, None] == slot_ids[None, None, :, :],
            slot_dots[None, None, :, :],
            0.0,
        ),
        axis=(2, 3),
    )
    center = jnp.sum(route_weight * weight_grad, axis=1, keepdims=True)
    logit_grad = route_weight * (weight_grad - center)
    matches = picks[:, :, None] == jnp.arange(every_expert, dtype=jnp.int32)[None, None, :]
    dense_grad = jnp.sum(jnp.where(matches, logit_grad[:, :, None], 0.0), axis=1)
    router_grad = jnp.zeros((token_count, width_model), jnp.float32)
    for part in split_bf16(dense_grad, 3):
        router_grad = router_grad + lax.dot_general(
            part, w_router, (((1,), (1,)), ((), ())), preferred_element_type=jnp.float32
        )
    expert_sum = jnp.zeros((token_count, width_model), jnp.float32)
    for part in split_bf16(combine, 2):
        expert_sum = expert_sum + jnp.einsum(
            "tes,esd->td", part, returned_rows, preferred_element_type=jnp.float32
        )
    grad_in = (incoming.astype(jnp.float32) + expert_sum + router_grad).astype(jnp.bfloat16)
    return (grad_in[None], logit_grad[None])


def solution(mesh):
    in_specs = (
        P("section", "expert", None),
        P("section", "expert", None),
        P("section", "expert", None),
        P("section", "expert", None),
        P("section", "expert", None, None),
        P("section", "expert", None, None),
        P("section", "expert", None, None),
        P("section", None, None),
    )
    out_specs = (P("section", "expert", None), P("section", "expert", None))
    return jax.shard_map(
        per_device, mesh=mesh, in_specs=in_specs, out_specs=out_specs, check_vma=False
    )
```

```python
import jax
import jax.numpy as jnp
from jax import lax
from jax.sharding import PartitionSpec as P


def from_behind(shard, axis, by):
    size = lax.axis_size(axis)
    return lax.ppermute(shard, axis, [(i, (i + by) % size) for i in range(size)])


def split_bf16(values, parts):
    pieces = []
    rest = values
    for _ in range(parts):
        piece = rest.astype(jnp.bfloat16)
        pieces.append(piece)
        rest = rest - piece.astype(jnp.float32)
    return pieces


def per_device(
    grad_out, layer_input, routes, route_logits, gate_weight, up_weight, down_weight, router_weight
):
    incoming = from_behind(grad_out, "section", -1)[0]
    x_in = layer_input[0]
    token_count, width_model = x_in.shape
    top_count = routes.shape[2]
    expert_count = lax.axis_size("expert")
    every_expert = router_weight.shape[2]
    capacity = 2 * token_count * top_count // every_expert
    slots_all = expert_count * capacity
    w_gate = gate_weight[0, 0]
    w_up = up_weight[0, 0]
    w_down = down_weight[0, 0]
    w_router = router_weight[0]
    picks = routes[0]

    experts = jnp.arange(expert_count, dtype=jnp.int32)
    hit = picks[:, :, None] == experts[None, None, :]
    per_token = jnp.sum(hit.astype(jnp.float32), axis=1).astype(jnp.bfloat16)
    token_ids = jnp.arange(token_count, dtype=jnp.int32)
    before = (token_ids[None, :] < token_ids[:, None]).astype(jnp.bfloat16)
    earlier = jnp.dot(before, per_token, preferred_element_type=jnp.float32).astype(jnp.int32)
    rank_inside = jnp.sum(jnp.where(hit, earlier[:, None, :], 0), axis=2)
    slot_index = jnp.where(picks < expert_count, picks * capacity + rank_inside, slots_all)

    exponent = jnp.exp(route_logits[0])
    route_weight = exponent / jnp.sum(exponent, axis=1, keepdims=True)

    slot_ids = jnp.arange(slots_all, dtype=jnp.int32).reshape(expert_count, capacity)
    pack = jnp.zeros((expert_count, capacity, token_count), jnp.float32)
    combine = jnp.zeros((token_count, expert_count, capacity), jnp.float32)
    for k in range(top_count):
        chosen = slot_index[:, k]
        pack = pack + (slot_ids[:, :, None] == chosen[None, None, :]).astype(jnp.float32)
        combine = combine + jnp.where(
            chosen[:, None, None] == slot_ids[None, :, :], route_weight[:, k][:, None, None], 0.0
        )
    pack = pack.astype(jnp.bfloat16)

    def pack_rows(rows):
        sent = jnp.einsum("est,td->esd", pack, rows, preferred_element_type=jnp.float32)
        return sent.astype(jnp.bfloat16)

    def exchange(block):
        return lax.all_to_all(block, "expert", split_axis=0, concat_axis=0, tiled=True)

    inputs = exchange(pack_rows(x_in))
    grad_rows = exchange(pack_rows(incoming))
    pre_gate = jnp.einsum("esd,df->esf", inputs, w_gate, preferred_element_type=jnp.float32)
    pre_up = jnp.einsum("esd,df->esf", inputs, w_up, preferred_element_type=jnp.float32)
    hidden_grad = jnp.einsum("esd,fd->esf", grad_rows, w_down, preferred_element_type=jnp.float32)
    sigmoid_gate = jax.nn.sigmoid(pre_gate)
    activation = pre_gate * sigmoid_gate
    pair_dots = jnp.sum(hidden_grad * activation * pre_up, axis=-1).astype(jnp.bfloat16)
    gate_grad = (
        hidden_grad * pre_up * sigmoid_gate * (1.0 + pre_gate * (1.0 - sigmoid_gate))
    ).astype(jnp.bfloat16)
    up_grad = (hidden_grad * activation).astype(jnp.bfloat16)
    pair_rows = jnp.einsum(
        "esf,df->esd", gate_grad, w_gate, preferred_element_type=jnp.float32
    ) + jnp.einsum("esf,df->esd", up_grad, w_up, preferred_element_type=jnp.float32)
    lanes = 128
    dot_lanes = jnp.where(
        jnp.arange(lanes, dtype=jnp.int32)[None, None, :] == 0, pair_dots[:, :, None], 0.0
    ).astype(jnp.bfloat16)
    returned = exchange(jnp.concatenate([pair_rows.astype(jnp.bfloat16), dot_lanes], axis=2))
    returned_rows = returned[:, :, :width_model]
    returned_dots = returned[:, :, width_model]

    slot_dots = returned_dots.astype(jnp.float32)
    weight_grad = jnp.sum(
        jnp.where(
            slot_index[:, :, None, None] == slot_ids[None, None, :, :],
            slot_dots[None, None, :, :],
            0.0,
        ),
        axis=(2, 3),
    )
    center = jnp.sum(route_weight * weight_grad, axis=1, keepdims=True)
    logit_grad = route_weight * (weight_grad - center)
    matches = picks[:, :, None] == jnp.arange(every_expert, dtype=jnp.int32)[None, None, :]
    dense_grad = jnp.sum(jnp.where(matches, logit_grad[:, :, None], 0.0), axis=1)
    router_grad = jnp.zeros((token_count, width_model), jnp.float32)
    for part in split_bf16(dense_grad, 3):
        router_grad = router_grad + lax.dot_general(
            part, w_router, (((1,), (1,)), ((), ())), preferred_element_type=jnp.float32
        )
    combine_parts = jnp.stack(split_bf16(combine, 2))
    expert_sum = jnp.sum(
        jnp.einsum("ptes,esd->ptd", combine_parts, returned_rows, preferred_element_type=jnp.float32),
        axis=0,
    )
    grad_in = (incoming.astype(jnp.float32) + expert_sum + router_grad).astype(jnp.bfloat16)
    return (grad_in[None], logit_grad[None])


def solution(mesh):
    in_specs = (
        P("section", "expert", None),
        P("section", "expert", None),
        P("section", "expert", None),
        P("section", "expert", None),
        P("section", "expert", None, None),
        P("section", "expert", None, None),
        P("section", "expert", None, None),
        P("section", None, None),
    )
    out_specs = (P("section", "expert", None), P("section", "expert", None))
    return jax.shard_map(
        per_device, mesh=mesh, in_specs=in_specs, out_specs=out_specs, check_vma=False
    )
```

```python
import jax
import jax.numpy as jnp
from jax import lax
from jax.sharding import PartitionSpec as P


def from_behind(shard, axis, by):
    size = lax.axis_size(axis)
    return lax.ppermute(shard, axis, [(i, (i + by) % size) for i in range(size)])


def split_bf16(values, parts):
    pieces = []
    rest = values
    for _ in range(parts):
        piece = rest.astype(jnp.bfloat16)
        pieces.append(piece)
        rest = rest - piece.astype(jnp.float32)
    return pieces


def per_device(
    grad_out, layer_input, routes, route_logits, gate_weight, up_weight, down_weight, router_weight
):
    incoming = from_behind(grad_out, "section", -1)[0]
    x_in = layer_input[0]
    token_count, width_model = x_in.shape
    top_count = routes.shape[2]
    expert_count = lax.axis_size("expert")
    every_expert = router_weight.shape[2]
    capacity = 2 * token_count * top_count // every_expert
    slots_all = expert_count * capacity
    w_gate = gate_weight[0, 0]
    w_up = up_weight[0, 0]
    w_down = down_weight[0, 0]
    w_router = router_weight[0]
    picks = routes[0]

    experts = jnp.arange(expert_count, dtype=jnp.int32)
    hit = picks[:, :, None] == experts[None, None, :]
    per_token = jnp.sum(hit.astype(jnp.float32), axis=1).astype(jnp.bfloat16)
    token_ids = jnp.arange(token_count, dtype=jnp.int32)
    before = (token_ids[None, :] < token_ids[:, None]).astype(jnp.bfloat16)
    earlier = jnp.dot(before, per_token, preferred_element_type=jnp.float32).astype(jnp.int32)
    rank_inside = jnp.sum(jnp.where(hit, earlier[:, None, :], 0), axis=2)
    slot_index = jnp.where(picks < expert_count, picks * capacity + rank_inside, slots_all)

    exponent = jnp.exp(route_logits[0])
    route_weight = exponent / jnp.sum(exponent, axis=1, keepdims=True)

    slot_ids = jnp.arange(slots_all, dtype=jnp.int32).reshape(expert_count, capacity)
    pack = jnp.zeros((expert_count, capacity, token_count), jnp.float32)
    combine = jnp.zeros((token_count, expert_count, capacity), jnp.float32)
    for k in range(top_count):
        chosen = slot_index[:, k]
        pack = pack + (slot_ids[:, :, None] == chosen[None, None, :]).astype(jnp.float32)
        combine = combine + jnp.where(
            chosen[:, None, None] == slot_ids[None, :, :], route_weight[:, k][:, None, None], 0.0
        )
    pack = pack.astype(jnp.bfloat16)

    def pack_rows(rows):
        sent = jnp.einsum("est,td->esd", pack, rows, preferred_element_type=jnp.float32)
        return sent.astype(jnp.bfloat16)

    def exchange(block):
        return lax.all_to_all(block, "expert", split_axis=0, concat_axis=0, tiled=True)

    got = exchange(pack_rows(jnp.concatenate([x_in, incoming], axis=1)))
    inputs = got[:, :, :width_model]
    grad_rows = got[:, :, width_model:]
    lanes = 128
    wide = width_model + lanes
    pad_cols = jnp.zeros((lanes, w_gate.shape[1]), w_gate.dtype)
    w_gate_wide = jnp.concatenate([w_gate, pad_cols], axis=0)
    w_up_wide = jnp.concatenate([w_up, pad_cols], axis=0)
    pre_gate = jnp.einsum("esd,df->esf", inputs, w_gate, preferred_element_type=jnp.float32)
    pre_up = jnp.einsum("esd,df->esf", inputs, w_up, preferred_element_type=jnp.float32)
    hidden_grad = jnp.einsum("esd,fd->esf", grad_rows, w_down, preferred_element_type=jnp.float32)
    sigmoid_gate = jax.nn.sigmoid(pre_gate)
    activation = pre_gate * sigmoid_gate
    pair_dots = jnp.sum(hidden_grad * activation * pre_up, axis=-1).astype(jnp.bfloat16)
    gate_grad = (
        hidden_grad * pre_up * sigmoid_gate * (1.0 + pre_gate * (1.0 - sigmoid_gate))
    ).astype(jnp.bfloat16)
    up_grad = (hidden_grad * activation).astype(jnp.bfloat16)
    pair_rows = jnp.einsum(
        "esf,df->esd", gate_grad, w_gate_wide, preferred_element_type=jnp.float32
    ) + jnp.einsum("esf,df->esd", up_grad, w_up_wide, preferred_element_type=jnp.float32)
    lane_ids = jnp.arange(wide, dtype=jnp.int32)[None, None, :]
    pair_rows = jnp.where(
        lane_ids == width_model, pair_dots.astype(jnp.float32)[:, :, None], pair_rows
    )
    returned = exchange(pair_rows.astype(jnp.bfloat16))
    returned_dots = returned[:, :, width_model]

    slot_dots = returned_dots.astype(jnp.float32)
    weight_grad = jnp.sum(
        jnp.where(
            slot_index[:, :, None, None] == slot_ids[None, None, :, :],
            slot_dots[None, None, :, :],
            0.0,
        ),
        axis=(2, 3),
    )
    center = jnp.sum(route_weight * weight_grad, axis=1, keepdims=True)
    logit_grad = route_weight * (weight_grad - center)
    matches = picks[:, :, None] == jnp.arange(every_expert, dtype=jnp.int32)[None, None, :]
    dense_grad = jnp.sum(jnp.where(matches, logit_grad[:, :, None], 0.0), axis=1)
    router_grad = jnp.zeros((token_count, width_model), jnp.float32)
    for part in split_bf16(dense_grad, 3):
        router_grad = router_grad + lax.dot_general(
            part, w_router, (((1,), (1,)), ((), ())), preferred_element_type=jnp.float32
        )
    combine_hi, combine_lo = split_bf16(combine, 2)
    expert_sum = jnp.einsum(
        "tes,esd->td", combine_hi, returned, preferred_element_type=jnp.float32
    ) + jnp.einsum("tes,esd->td", combine_lo, returned, preferred_element_type=jnp.float32)
    expert_sum = expert_sum[:, :width_model]
    grad_in = (incoming.astype(jnp.float32) + expert_sum + router_grad).astype(jnp.bfloat16)
    return (grad_in[None], logit_grad[None])


def solution(mesh):
    in_specs = (
        P("section", "expert", None),
        P("section", "expert", None),
        P("section", "expert", None),
        P("section", "expert", None),
        P("section", "expert", None, None),
        P("section", "expert", None, None),
        P("section", "expert", None, None),
        P("section", None, None),
    )
    out_specs = (P("section", "expert", None), P("section", "expert", None))
    return jax.shard_map(
        per_device, mesh=mesh, in_specs=in_specs, out_specs=out_specs, check_vma=False
    )
```

```python
import jax
import jax.numpy as jnp
from jax import lax
from jax.sharding import PartitionSpec as P


def from_behind(shard, axis, by):
    size = lax.axis_size(axis)
    return lax.ppermute(shard, axis, [(i, (i + by) % size) for i in range(size)])


def split_bf16(values, parts):
    pieces = []
    rest = values
    for _ in range(parts):
        piece = rest.astype(jnp.bfloat16)
        pieces.append(piece)
        rest = rest - piece.astype(jnp.float32)
    return pieces


def per_device(
    grad_out, layer_input, routes, route_logits, gate_weight, up_weight, down_weight, router_weight
):
    row_blocks = 4 if grad_out.shape[1] % 64 == 0 else 1
    block_rows = grad_out.shape[1] // row_blocks
    incoming = jnp.concatenate(
        [
            from_behind(grad_out[0, b * block_rows : (b + 1) * block_rows], "section", -1)
            for b in range(row_blocks)
        ],
        axis=0,
    )
    x_in = layer_input[0]
    token_count, width_model = x_in.shape
    top_count = routes.shape[2]
    expert_count = lax.axis_size("expert")
    every_expert = router_weight.shape[2]
    capacity = 2 * token_count * top_count // every_expert
    slots_all = expert_count * capacity
    w_gate = gate_weight[0, 0]
    w_up = up_weight[0, 0]
    w_down = down_weight[0, 0]
    w_router = router_weight[0]
    picks = routes[0]

    experts = jnp.arange(expert_count, dtype=jnp.int32)
    hit = picks[:, :, None] == experts[None, None, :]
    per_token = jnp.sum(hit.astype(jnp.float32), axis=1).astype(jnp.bfloat16)
    token_ids = jnp.arange(token_count, dtype=jnp.int32)
    before = (token_ids[None, :] < token_ids[:, None]).astype(jnp.bfloat16)
    earlier = jnp.dot(before, per_token, preferred_element_type=jnp.float32).astype(jnp.int32)
    rank_inside = jnp.sum(jnp.where(hit, earlier[:, None, :], 0), axis=2)
    slot_index = jnp.where(picks < expert_count, picks * capacity + rank_inside, slots_all)

    exponent = jnp.exp(route_logits[0])
    route_weight = exponent / jnp.sum(exponent, axis=1, keepdims=True)

    slot_ids = jnp.arange(slots_all, dtype=jnp.int32).reshape(expert_count, capacity)
    pack = jnp.zeros((expert_count, capacity, token_count), jnp.float32)
    combine = jnp.zeros((token_count, expert_count, capacity), jnp.float32)
    for k in range(top_count):
        chosen = slot_index[:, k]
        pack = pack + (slot_ids[:, :, None] == chosen[None, None, :]).astype(jnp.float32)
        combine = combine + jnp.where(
            chosen[:, None, None] == slot_ids[None, :, :], route_weight[:, k][:, None, None], 0.0
        )
    pack = pack.astype(jnp.bfloat16)

    def pack_rows(rows):
        sent = jnp.einsum("est,td->esd", pack, rows, preferred_element_type=jnp.float32)
        return sent.astype(jnp.bfloat16)

    def exchange(block):
        return lax.all_to_all(block, "expert", split_axis=0, concat_axis=0, tiled=True)

    got = exchange(pack_rows(jnp.concatenate([x_in, incoming], axis=1)))
    inputs = got[:, :, :width_model]
    grad_rows = got[:, :, width_model:]
    lanes = 128
    wide = width_model + lanes
    pad_cols = jnp.zeros((lanes, w_gate.shape[1]), w_gate.dtype)
    w_gate_wide = jnp.concatenate([w_gate, pad_cols], axis=0)
    w_up_wide = jnp.concatenate([w_up, pad_cols], axis=0)
    hidden_count = w_gate.shape[1]
    pre_both = jnp.einsum(
        "esd,df->esf", inputs, jnp.concatenate([w_gate, w_up], axis=1),
        preferred_element_type=jnp.float32,
    )
    pre_gate = pre_both[:, :, :hidden_count]
    pre_up = pre_both[:, :, hidden_count:]
    hidden_grad = jnp.einsum("esd,fd->esf", grad_rows, w_down, preferred_element_type=jnp.float32)
    sigmoid_gate = jax.nn.sigmoid(pre_gate)
    activation = pre_gate * sigmoid_gate
    pair_dots = jnp.sum(hidden_grad * activation * pre_up, axis=-1).astype(jnp.bfloat16)
    gate_grad = (
        hidden_grad * pre_up * sigmoid_gate * (1.0 + pre_gate * (1.0 - sigmoid_gate))
    ).astype(jnp.bfloat16)
    up_grad = (hidden_grad * activation).astype(jnp.bfloat16)
    pair_rows = jnp.einsum(
        "esf,df->esd", gate_grad, w_gate_wide, preferred_element_type=jnp.float32
    ) + jnp.einsum("esf,df->esd", up_grad, w_up_wide, preferred_element_type=jnp.float32)
    lane_ids = jnp.arange(wide, dtype=jnp.int32)[None, None, :]
    pair_rows = jnp.where(
        lane_ids == width_model, pair_dots.astype(jnp.float32)[:, :, None], pair_rows
    )
    returned = exchange(pair_rows.astype(jnp.bfloat16))
    returned_dots = returned[:, :, width_model]

    slot_dots = returned_dots.astype(jnp.float32)
    weight_grad = jnp.sum(
        jnp.where(
            slot_index[:, :, None, None] == slot_ids[None, None, :, :],
            slot_dots[None, None, :, :],
            0.0,
        ),
        axis=(2, 3),
    )
    center = jnp.sum(route_weight * weight_grad, axis=1, keepdims=True)
    logit_grad = route_weight * (weight_grad - center)
    matches = picks[:, :, None] == jnp.arange(every_expert, dtype=jnp.int32)[None, None, :]
    dense_grad = jnp.sum(jnp.where(matches, logit_grad[:, :, None], 0.0), axis=1)
    router_grad = jnp.zeros((token_count, width_model), jnp.float32)
    for part in split_bf16(dense_grad, 3):
        router_grad = router_grad + lax.dot_general(
            part, w_router, (((1,), (1,)), ((), ())), preferred_element_type=jnp.float32
        )
    combine_parts = jnp.stack(split_bf16(combine, 2))
    expert_both = jnp.einsum(
        "ptes,esd->ptd", combine_parts, returned, preferred_element_type=jnp.float32
    )
    expert_sum = expert_both[0, :, :width_model] + expert_both[1, :, :width_model]
    grad_in = (incoming.astype(jnp.float32) + expert_sum + router_grad).astype(jnp.bfloat16)
    return (grad_in[None], logit_grad[None])


def solution(mesh):
    in_specs = (
        P("section", "expert", None),
        P("section", "expert", None),
        P("section", "expert", None),
        P("section", "expert", None),
        P("section", "expert", None, None),
        P("section", "expert", None, None),
        P("section", "expert", None, None),
        P("section", None, None),
    )
    out_specs = (P("section", "expert", None), P("section", "expert", None))
    return jax.shard_map(
        per_device, mesh=mesh, in_specs=in_specs, out_specs=out_specs, check_vma=False
    )
```

```python
import jax
import jax.numpy as jnp
from jax import lax
from jax.sharding import PartitionSpec as P


def from_behind(shard, axis, by):
    size = lax.axis_size(axis)
    return lax.ppermute(shard, axis, [(i, (i + by) % size) for i in range(size)])


def split_bf16(values, parts):
    pieces = []
    rest = values
    for _ in range(parts):
        piece = rest.astype(jnp.bfloat16)
        pieces.append(piece)
        rest = rest - piece.astype(jnp.float32)
    return pieces


def per_device(
    grad_out, layer_input, routes, route_logits, gate_weight, up_weight, down_weight, router_weight
):
    incoming = from_behind(grad_out, "section", -1)[0]
    x_in = layer_input[0]
    token_count, width_model = x_in.shape
    top_count = routes.shape[2]
    expert_count = lax.axis_size("expert")
    every_expert = router_weight.shape[2]
    capacity = 2 * token_count * top_count // every_expert
    slots_all = expert_count * capacity
    w_gate = gate_weight[0, 0]
    w_up = up_weight[0, 0]
    w_down = down_weight[0, 0]
    w_router = router_weight[0]
    picks = routes[0]

    experts = jnp.arange(expert_count, dtype=jnp.int32)
    hit = picks[:, :, None] == experts[None, None, :]
    per_token = jnp.sum(hit.astype(jnp.float32), axis=1).astype(jnp.bfloat16)
    token_ids = jnp.arange(token_count, dtype=jnp.int32)
    before = (token_ids[None, :] < token_ids[:, None]).astype(jnp.bfloat16)
    earlier = jnp.dot(before, per_token, preferred_element_type=jnp.float32).astype(jnp.int32)
    rank_inside = jnp.sum(jnp.where(hit, earlier[:, None, :], 0), axis=2)
    slot_index = jnp.where(picks < expert_count, picks * capacity + rank_inside, slots_all)

    exponent = jnp.exp(route_logits[0])
    route_weight = exponent / jnp.sum(exponent, axis=1, keepdims=True)

    slot_ids = jnp.arange(slots_all, dtype=jnp.int32).reshape(expert_count, capacity)
    pack = jnp.zeros((expert_count, capacity, token_count), jnp.float32)
    combine = jnp.zeros((token_count, expert_count, capacity), jnp.float32)
    for k in range(top_count):
        chosen = slot_index[:, k]
        pack = pack + (slot_ids[:, :, None] == chosen[None, None, :]).astype(jnp.float32)
        combine = combine + jnp.where(
            chosen[:, None, None] == slot_ids[None, :, :], route_weight[:, k][:, None, None], 0.0
        )
    pack = pack.astype(jnp.bfloat16)

    def pack_rows(rows):
        sent = jnp.einsum("est,td->esd", pack, rows, preferred_element_type=jnp.float32)
        return sent.astype(jnp.bfloat16)

    def exchange(block):
        return lax.all_to_all(block, "expert", split_axis=0, concat_axis=0, tiled=True)

    got = exchange(pack_rows(jnp.concatenate([x_in, incoming], axis=1)))
    inputs = got[:, :, :width_model]
    grad_rows = got[:, :, width_model:]
    lanes = 128
    wide = width_model + lanes
    pad_cols = jnp.zeros((lanes, w_gate.shape[1]), w_gate.dtype)
    w_gate_wide = jnp.concatenate([w_gate, pad_cols], axis=0)
    w_up_wide = jnp.concatenate([w_up, pad_cols], axis=0)
    hidden_count = w_gate.shape[1]
    pre_both = jnp.einsum(
        "esd,df->esf", inputs, jnp.concatenate([w_gate, w_up], axis=1),
        preferred_element_type=jnp.float32,
    )
    pre_gate = pre_both[:, :, :hidden_count]
    pre_up = pre_both[:, :, hidden_count:]
    hidden_grad = jnp.einsum("esd,fd->esf", grad_rows, w_down, preferred_element_type=jnp.float32)
    sigmoid_gate = jax.nn.sigmoid(pre_gate)
    activation = pre_gate * sigmoid_gate
    pair_dots = jnp.sum(hidden_grad * activation * pre_up, axis=-1).astype(jnp.bfloat16)
    gate_grad = (
        hidden_grad * pre_up * sigmoid_gate * (1.0 + pre_gate * (1.0 - sigmoid_gate))
    ).astype(jnp.bfloat16)
    up_grad = (hidden_grad * activation).astype(jnp.bfloat16)
    pair_rows = jnp.einsum(
        "esf,df->esd", gate_grad, w_gate_wide, preferred_element_type=jnp.float32
    ) + jnp.einsum("esf,df->esd", up_grad, w_up_wide, preferred_element_type=jnp.float32)
    lane_ids = jnp.arange(wide, dtype=jnp.int32)[None, None, :]
    pair_rows = jnp.where(
        lane_ids == width_model, pair_dots.astype(jnp.float32)[:, :, None], pair_rows
    )
    returned = exchange(pair_rows.astype(jnp.bfloat16))
    returned_dots = returned[:, :, width_model]

    slot_dots = returned_dots.astype(jnp.float32)
    weight_grad = jnp.sum(
        jnp.where(
            slot_index[:, :, None, None] == slot_ids[None, None, :, :],
            slot_dots[None, None, :, :],
            0.0,
        ),
        axis=(2, 3),
    )
    center = jnp.sum(route_weight * weight_grad, axis=1, keepdims=True)
    logit_grad = route_weight * (weight_grad - center)
    matches = picks[:, :, None] == jnp.arange(every_expert, dtype=jnp.int32)[None, None, :]
    dense_grad = jnp.sum(jnp.where(matches, logit_grad[:, :, None], 0.0), axis=1)
    router_grad = jnp.zeros((token_count, width_model), jnp.float32)
    for part in split_bf16(dense_grad, 3):
        router_grad = router_grad + lax.dot_general(
            part, w_router, (((1,), (1,)), ((), ())), preferred_element_type=jnp.float32
        )
    combine_parts = jnp.stack(split_bf16(combine, 2))
    expert_both = jnp.einsum(
        "ptes,esd->ptd", combine_parts, returned, preferred_element_type=jnp.float32
    )
    expert_sum = expert_both[0, :, :width_model] + expert_both[1, :, :width_model]
    grad_in = (incoming.astype(jnp.float32) + expert_sum + router_grad).astype(jnp.bfloat16)
    return (grad_in[None], logit_grad[None])


def solution(mesh):
    in_specs = (
        P("section", "expert", None),
        P("section", "expert", None),
        P("section", "expert", None),
        P("section", "expert", None),
        P("section", "expert", None, None),
        P("section", "expert", None, None),
        P("section", "expert", None, None),
        P("section", None, None),
    )
    out_specs = (P("section", "expert", None), P("section", "expert", None))
    return jax.shard_map(
        per_device, mesh=mesh, in_specs=in_specs, out_specs=out_specs, check_vma=False
    )
```

```python
import jax
import jax.numpy as jnp
from jax import lax
from jax.sharding import PartitionSpec as P


def from_behind(shard, axis, by):
    size = lax.axis_size(axis)
    return lax.ppermute(shard, axis, [(i, (i + by) % size) for i in range(size)])


def split_bf16(values, parts):
    pieces = []
    rest = values
    for _ in range(parts):
        piece = rest.astype(jnp.bfloat16)
        pieces.append(piece)
        rest = rest - piece.astype(jnp.float32)
    return pieces


def per_device(
    grad_out, layer_input, routes, route_logits, gate_weight, up_weight, down_weight, router_weight
):
    incoming = from_behind(grad_out, "section", -1)[0]
    x_in = layer_input[0]
    token_count, width_model = x_in.shape
    top_count = routes.shape[2]
    expert_count = lax.axis_size("expert")
    every_expert = router_weight.shape[2]
    capacity = 2 * token_count * top_count // every_expert
    slots_all = expert_count * capacity
    w_gate = gate_weight[0, 0]
    w_up = up_weight[0, 0]
    w_down = down_weight[0, 0]
    w_router = router_weight[0]
    picks = routes[0]

    experts = jnp.arange(expert_count, dtype=jnp.int32)
    hit = picks[:, :, None] == experts[None, None, :]
    per_token = jnp.sum(hit.astype(jnp.float32), axis=1).astype(jnp.bfloat16)
    token_ids = jnp.arange(token_count, dtype=jnp.int32)
    before = (token_ids[None, :] < token_ids[:, None]).astype(jnp.bfloat16)
    earlier = jnp.dot(before, per_token, preferred_element_type=jnp.float32).astype(jnp.int32)
    rank_inside = jnp.sum(jnp.where(hit, earlier[:, None, :], 0), axis=2)
    slot_index = jnp.where(picks < expert_count, picks * capacity + rank_inside, slots_all)

    exponent = jnp.exp(route_logits[0])
    route_weight = exponent / jnp.sum(exponent, axis=1, keepdims=True)

    slot_ids = jnp.arange(slots_all, dtype=jnp.int32).reshape(expert_count, capacity)
    pack = jnp.zeros((expert_count, capacity, token_count), jnp.float32)
    combine = jnp.zeros((token_count, expert_count, capacity), jnp.float32)
    for k in range(top_count):
        chosen = slot_index[:, k]
        pack = pack + (slot_ids[:, :, None] == chosen[None, None, :]).astype(jnp.float32)
        combine = combine + jnp.where(
            chosen[:, None, None] == slot_ids[None, :, :], route_weight[:, k][:, None, None], 0.0
        )
    pack = pack.astype(jnp.bfloat16)
    combine_parts = jnp.stack(split_bf16(combine, 2))
    pack, combine_parts = lax.optimization_barrier((pack, combine_parts))

    def pack_rows(rows):
        sent = jnp.einsum("est,td->esd", pack, rows, preferred_element_type=jnp.float32)
        return sent.astype(jnp.bfloat16)

    def exchange(block):
        return lax.all_to_all(block, "expert", split_axis=0, concat_axis=0, tiled=True)

    got = exchange(pack_rows(jnp.concatenate([x_in, incoming], axis=1)))
    inputs = got[:, :, :width_model]
    grad_rows = got[:, :, width_model:]
    lanes = 128
    wide = width_model + lanes
    pad_cols = jnp.zeros((lanes, w_gate.shape[1]), w_gate.dtype)
    w_gate_wide = jnp.concatenate([w_gate, pad_cols], axis=0)
    w_up_wide = jnp.concatenate([w_up, pad_cols], axis=0)
    hidden_count = w_gate.shape[1]
    pre_both = jnp.einsum(
        "esd,df->esf", inputs, jnp.concatenate([w_gate, w_up], axis=1),
        preferred_element_type=jnp.float32,
    )
    pre_gate = pre_both[:, :, :hidden_count]
    pre_up = pre_both[:, :, hidden_count:]
    hidden_grad = jnp.einsum("esd,fd->esf", grad_rows, w_down, preferred_element_type=jnp.float32)
    sigmoid_gate = jax.nn.sigmoid(pre_gate)
    activation = pre_gate * sigmoid_gate
    pair_dots = jnp.sum(hidden_grad * activation * pre_up, axis=-1).astype(jnp.bfloat16)
    gate_grad = (
        hidden_grad * pre_up * sigmoid_gate * (1.0 + pre_gate * (1.0 - sigmoid_gate))
    ).astype(jnp.bfloat16)
    up_grad = (hidden_grad * activation).astype(jnp.bfloat16)
    pair_rows = jnp.einsum(
        "esf,df->esd", gate_grad, w_gate_wide, preferred_element_type=jnp.float32
    ) + jnp.einsum("esf,df->esd", up_grad, w_up_wide, preferred_element_type=jnp.float32)
    lane_ids = jnp.arange(wide, dtype=jnp.int32)[None, None, :]
    pair_rows = jnp.where(
        lane_ids == width_model, pair_dots.astype(jnp.float32)[:, :, None], pair_rows
    )
    returned = exchange(pair_rows.astype(jnp.bfloat16))
    returned_dots = returned[:, :, width_model]

    slot_dots = returned_dots.astype(jnp.float32)
    weight_grad = jnp.sum(
        jnp.where(
            slot_index[:, :, None, None] == slot_ids[None, None, :, :],
            slot_dots[None, None, :, :],
            0.0,
        ),
        axis=(2, 3),
    )
    center = jnp.sum(route_weight * weight_grad, axis=1, keepdims=True)
    logit_grad = route_weight * (weight_grad - center)
    matches = picks[:, :, None] == jnp.arange(every_expert, dtype=jnp.int32)[None, None, :]
    dense_grad = jnp.sum(jnp.where(matches, logit_grad[:, :, None], 0.0), axis=1)
    router_grad = jnp.zeros((token_count, width_model), jnp.float32)
    for part in split_bf16(dense_grad, 3):
        router_grad = router_grad + lax.dot_general(
            part, w_router, (((1,), (1,)), ((), ())), preferred_element_type=jnp.float32
        )
    expert_both = jnp.einsum(
        "ptes,esd->ptd", combine_parts, returned, preferred_element_type=jnp.float32
    )
    expert_sum = expert_both[0, :, :width_model] + expert_both[1, :, :width_model]
    grad_in = (incoming.astype(jnp.float32) + expert_sum + router_grad).astype(jnp.bfloat16)
    return (grad_in[None], logit_grad[None])


def solution(mesh):
    in_specs = (
        P("section", "expert", None),
        P("section", "expert", None),
        P("section", "expert", None),
        P("section", "expert", None),
        P("section", "expert", None, None),
        P("section", "expert", None, None),
        P("section", "expert", None, None),
        P("section", None, None),
    )
    out_specs = (P("section", "expert", None), P("section", "expert", None))
    return jax.shard_map(
        per_device, mesh=mesh, in_specs=in_specs, out_specs=out_specs, check_vma=False
    )
```

```python
import jax
import jax.numpy as jnp
from jax import lax
from jax.sharding import PartitionSpec as P


def from_behind(shard, axis, by):
    size = lax.axis_size(axis)
    return lax.ppermute(shard, axis, [(i, (i + by) % size) for i in range(size)])


def split_bf16(values, parts):
    pieces = []
    rest = values
    for _ in range(parts):
        piece = rest.astype(jnp.bfloat16)
        pieces.append(piece)
        rest = rest - piece.astype(jnp.float32)
    return pieces


def per_device(
    grad_out, layer_input, routes, route_logits, gate_weight, up_weight, down_weight, router_weight
):
    incoming = from_behind(grad_out, "section", -1)[0]
    x_in = layer_input[0]
    token_count, width_model = x_in.shape
    top_count = routes.shape[2]
    expert_count = lax.axis_size("expert")
    every_expert = router_weight.shape[2]
    capacity = 2 * token_count * top_count // every_expert
    slots_all = expert_count * capacity
    w_gate = gate_weight[0, 0]
    w_up = up_weight[0, 0]
    w_down = down_weight[0, 0]
    w_router = router_weight[0]
    picks = routes[0]

    experts = jnp.arange(expert_count, dtype=jnp.int32)
    hit = picks[:, :, None] == experts[None, None, :]
    per_token = jnp.sum(hit.astype(jnp.float32), axis=1).astype(jnp.bfloat16)
    token_ids = jnp.arange(token_count, dtype=jnp.int32)
    before = (token_ids[None, :] < token_ids[:, None]).astype(jnp.bfloat16)
    earlier = jnp.dot(before, per_token, preferred_element_type=jnp.float32).astype(jnp.int32)
    rank_inside = jnp.sum(jnp.where(hit, earlier[:, None, :], 0), axis=2)
    slot_index = jnp.where(picks < expert_count, picks * capacity + rank_inside, slots_all)

    exponent = jnp.exp(route_logits[0])
    route_weight = exponent / jnp.sum(exponent, axis=1, keepdims=True)

    slot_ids = jnp.arange(slots_all, dtype=jnp.int32).reshape(expert_count, capacity)
    pack = jnp.zeros((expert_count, capacity, token_count), jnp.float32)
    combine = jnp.zeros((token_count, expert_count, capacity), jnp.float32)
    for k in range(top_count):
        chosen = slot_index[:, k]
        pack = pack + (slot_ids[:, :, None] == chosen[None, None, :]).astype(jnp.float32)
        combine = combine + jnp.where(
            chosen[:, None, None] == slot_ids[None, :, :], route_weight[:, k][:, None, None], 0.0
        )
    pack = pack.astype(jnp.bfloat16)
    combine_parts = jnp.stack(split_bf16(combine, 2))
    pack, combine_parts = lax.optimization_barrier((pack, combine_parts))

    def pack_rows(rows):
        sent = jnp.einsum("est,td->esd", pack, rows, preferred_element_type=jnp.float32)
        return sent.astype(jnp.bfloat16)

    def exchange(block):
        return lax.all_to_all(block, "expert", split_axis=0, concat_axis=0, tiled=True)

    got = exchange(pack_rows(jnp.concatenate([x_in, incoming], axis=1)))
    inputs = got[:, :, :width_model]
    grad_rows = got[:, :, width_model:]
    lanes = 128
    wide = width_model + lanes
    pad_cols = jnp.zeros((lanes, w_gate.shape[1]), w_gate.dtype)
    w_gate_wide = jnp.concatenate([w_gate, pad_cols], axis=0)
    w_up_wide = jnp.concatenate([w_up, pad_cols], axis=0)
    hidden_count = w_gate.shape[1]
    pre_both = jnp.einsum(
        "esd,df->esf", inputs, jnp.concatenate([w_gate, w_up], axis=1),
        preferred_element_type=jnp.float32,
    )
    pre_gate = pre_both[:, :, :hidden_count]
    pre_up = pre_both[:, :, hidden_count:]
    hidden_grad = jnp.einsum("esd,fd->esf", grad_rows, w_down, preferred_element_type=jnp.float32)
    sigmoid_gate = jax.nn.sigmoid(pre_gate)
    activation = pre_gate * sigmoid_gate
    pair_dots = jnp.sum(hidden_grad * activation * pre_up, axis=-1).astype(jnp.bfloat16)
    gate_grad = (
        hidden_grad * pre_up * sigmoid_gate * (1.0 + pre_gate * (1.0 - sigmoid_gate))
    ).astype(jnp.bfloat16)
    up_grad = (hidden_grad * activation).astype(jnp.bfloat16)
    pair_rows = jnp.einsum(
        "esf,df->esd",
        jnp.concatenate([gate_grad, up_grad], axis=2),
        jnp.concatenate([w_gate_wide, w_up_wide], axis=1),
        preferred_element_type=jnp.float32,
    )
    lane_ids = jnp.arange(wide, dtype=jnp.int32)[None, None, :]
    pair_rows = jnp.where(
        lane_ids == width_model, pair_dots.astype(jnp.float32)[:, :, None], pair_rows
    )
    returned = exchange(pair_rows.astype(jnp.bfloat16))
    returned_dots = returned[:, :, width_model]

    slot_dots = returned_dots.astype(jnp.float32)
    weight_grad = jnp.sum(
        jnp.where(
            slot_index[:, :, None, None] == slot_ids[None, None, :, :],
            slot_dots[None, None, :, :],
            0.0,
        ),
        axis=(2, 3),
    )
    center = jnp.sum(route_weight * weight_grad, axis=1, keepdims=True)
    logit_grad = route_weight * (weight_grad - center)
    matches = picks[:, :, None] == jnp.arange(every_expert, dtype=jnp.int32)[None, None, :]
    dense_grad = jnp.sum(jnp.where(matches, logit_grad[:, :, None], 0.0), axis=1)
    router_grad = jnp.zeros((token_count, width_model), jnp.float32)
    for part in split_bf16(dense_grad, 3):
        router_grad = router_grad + lax.dot_general(
            part, w_router, (((1,), (1,)), ((), ())), preferred_element_type=jnp.float32
        )
    expert_both = jnp.einsum(
        "ptes,esd->ptd", combine_parts, returned, preferred_element_type=jnp.float32
    )
    expert_sum = expert_both[0, :, :width_model] + expert_both[1, :, :width_model]
    grad_in = (incoming.astype(jnp.float32) + expert_sum + router_grad).astype(jnp.bfloat16)
    return (grad_in[None], logit_grad[None])


def solution(mesh):
    in_specs = (
        P("section", "expert", None),
        P("section", "expert", None),
        P("section", "expert", None),
        P("section", "expert", None),
        P("section", "expert", None, None),
        P("section", "expert", None, None),
        P("section", "expert", None, None),
        P("section", None, None),
    )
    out_specs = (P("section", "expert", None), P("section", "expert", None))
    return jax.shard_map(
        per_device, mesh=mesh, in_specs=in_specs, out_specs=out_specs, check_vma=False
    )
```

```python
import jax
import jax.numpy as jnp
from jax import lax
from jax.sharding import PartitionSpec as P


def from_behind(shard, axis, by):
    size = lax.axis_size(axis)
    return lax.ppermute(shard, axis, [(i, (i + by) % size) for i in range(size)])


def split_bf16(values, parts):
    pieces = []
    rest = values
    for _ in range(parts):
        piece = rest.astype(jnp.bfloat16)
        pieces.append(piece)
        rest = rest - piece.astype(jnp.float32)
    return pieces


def per_device(
    grad_out, layer_input, routes, route_logits, gate_weight, up_weight, down_weight, router_weight
):
    incoming = from_behind(grad_out, "section", -1)[0]
    x_in = layer_input[0]
    token_count, width_model = x_in.shape
    top_count = routes.shape[2]
    expert_count = lax.axis_size("expert")
    every_expert = router_weight.shape[2]
    capacity = 2 * token_count * top_count // every_expert
    slots_all = expert_count * capacity
    w_gate = gate_weight[0, 0]
    w_up = up_weight[0, 0]
    w_down = down_weight[0, 0]
    w_router = router_weight[0]
    picks = routes[0]

    experts = jnp.arange(expert_count, dtype=jnp.int32)
    hit = picks[:, :, None] == experts[None, None, :]
    per_token = jnp.sum(hit.astype(jnp.float32), axis=1).astype(jnp.bfloat16)
    token_ids = jnp.arange(token_count, dtype=jnp.int32)
    before = (token_ids[None, :] < token_ids[:, None]).astype(jnp.bfloat16)
    earlier = jnp.dot(before, per_token, preferred_element_type=jnp.float32).astype(jnp.int32)
    rank_inside = jnp.sum(jnp.where(hit, earlier[:, None, :], 0), axis=2)
    slot_index = jnp.where(picks < expert_count, picks * capacity + rank_inside, slots_all)

    exponent = jnp.exp(route_logits[0])
    route_weight = exponent / jnp.sum(exponent, axis=1, keepdims=True)

    slot_ids = jnp.arange(slots_all, dtype=jnp.int32).reshape(expert_count, capacity)
    pack = jnp.zeros((expert_count, capacity, token_count), jnp.float32)
    combine = jnp.zeros((token_count, expert_count, capacity), jnp.float32)
    for k in range(top_count):
        chosen = slot_index[:, k]
        pack = pack + (slot_ids[:, :, None] == chosen[None, None, :]).astype(jnp.float32)
        combine = combine + jnp.where(
            chosen[:, None, None] == slot_ids[None, :, :], route_weight[:, k][:, None, None], 0.0
        )
    pack = pack.astype(jnp.bfloat16)
    combine_parts = jnp.stack(split_bf16(combine, 2))
    pack, combine_parts = lax.optimization_barrier((pack, combine_parts))

    def pack_rows(rows):
        sent = jnp.einsum("est,td->esd", pack, rows, preferred_element_type=jnp.float32)
        return sent.astype(jnp.bfloat16)

    def exchange(block):
        return lax.all_to_all(block, "expert", split_axis=0, concat_axis=0, tiled=True)

    sent = jnp.concatenate([pack_rows(x_in), jnp.zeros_like(pack_rows(x_in))], axis=2)
    sent = lax.optimization_barrier(sent)
    got = exchange(lax.dynamic_update_slice(sent, pack_rows(incoming), (0, 0, width_model)))
    inputs = got[:, :, :width_model]
    grad_rows = got[:, :, width_model:]
    lanes = 128
    wide = width_model + lanes
    pad_cols = jnp.zeros((lanes, w_gate.shape[1]), w_gate.dtype)
    w_gate_wide = jnp.concatenate([w_gate, pad_cols], axis=0)
    w_up_wide = jnp.concatenate([w_up, pad_cols], axis=0)
    hidden_count = w_gate.shape[1]
    pre_both = jnp.einsum(
        "esd,df->esf", inputs, jnp.concatenate([w_gate, w_up], axis=1),
        preferred_element_type=jnp.float32,
    )
    pre_gate = pre_both[:, :, :hidden_count]
    pre_up = pre_both[:, :, hidden_count:]
    hidden_grad = jnp.einsum("esd,fd->esf", grad_rows, w_down, preferred_element_type=jnp.float32)
    sigmoid_gate = jax.nn.sigmoid(pre_gate)
    activation = pre_gate * sigmoid_gate
    pair_dots = jnp.sum(hidden_grad * activation * pre_up, axis=-1).astype(jnp.bfloat16)
    gate_grad = (
        hidden_grad * pre_up * sigmoid_gate * (1.0 + pre_gate * (1.0 - sigmoid_gate))
    ).astype(jnp.bfloat16)
    up_grad = (hidden_grad * activation).astype(jnp.bfloat16)
    pair_rows = jnp.einsum(
        "esf,df->esd", gate_grad, w_gate_wide, preferred_element_type=jnp.float32
    ) + jnp.einsum("esf,df->esd", up_grad, w_up_wide, preferred_element_type=jnp.float32)
    lane_ids = jnp.arange(wide, dtype=jnp.int32)[None, None, :]
    pair_rows = jnp.where(
        lane_ids == width_model, pair_dots.astype(jnp.float32)[:, :, None], pair_rows
    )
    returned = exchange(pair_rows.astype(jnp.bfloat16))
    returned_dots = returned[:, :, width_model]

    slot_dots = returned_dots.astype(jnp.float32)
    weight_grad = jnp.sum(
        jnp.where(
            slot_index[:, :, None, None] == slot_ids[None, None, :, :],
            slot_dots[None, None, :, :],
            0.0,
        ),
        axis=(2, 3),
    )
    center = jnp.sum(route_weight * weight_grad, axis=1, keepdims=True)
    logit_grad = route_weight * (weight_grad - center)
    matches = picks[:, :, None] == jnp.arange(every_expert, dtype=jnp.int32)[None, None, :]
    dense_grad = jnp.sum(jnp.where(matches, logit_grad[:, :, None], 0.0), axis=1)
    router_grad = jnp.zeros((token_count, width_model), jnp.float32)
    for part in split_bf16(dense_grad, 3):
        router_grad = router_grad + lax.dot_general(
            part, w_router, (((1,), (1,)), ((), ())), preferred_element_type=jnp.float32
        )
    expert_both = jnp.einsum(
        "ptes,esd->ptd", combine_parts, returned, preferred_element_type=jnp.float32
    )
    expert_sum = expert_both[0, :, :width_model] + expert_both[1, :, :width_model]
    grad_in = (incoming.astype(jnp.float32) + expert_sum + router_grad).astype(jnp.bfloat16)
    return (grad_in[None], logit_grad[None])


def solution(mesh):
    in_specs = (
        P("section", "expert", None),
        P("section", "expert", None),
        P("section", "expert", None),
        P("section", "expert", None),
        P("section", "expert", None, None),
        P("section", "expert", None, None),
        P("section", "expert", None, None),
        P("section", None, None),
    )
    out_specs = (P("section", "expert", None), P("section", "expert", None))
    return jax.shard_map(
        per_device, mesh=mesh, in_specs=in_specs, out_specs=out_specs, check_vma=False
    )
```

```python
import jax
import jax.numpy as jnp
from jax import lax
from jax.sharding import PartitionSpec as P


def from_behind(shard, axis, by):
    size = lax.axis_size(axis)
    return lax.ppermute(shard, axis, [(i, (i + by) % size) for i in range(size)])


def split_bf16(values, parts):
    pieces = []
    rest = values
    for _ in range(parts):
        piece = rest.astype(jnp.bfloat16)
        pieces.append(piece)
        rest = rest - piece.astype(jnp.float32)
    return pieces


def per_device(
    grad_out, layer_input, routes, route_logits, gate_weight, up_weight, down_weight, router_weight
):
    incoming = from_behind(grad_out, "section", -1)[0]
    x_in = layer_input[0]
    token_count, width_model = x_in.shape
    top_count = routes.shape[2]
    expert_count = lax.axis_size("expert")
    every_expert = router_weight.shape[2]
    capacity = 2 * token_count * top_count // every_expert
    slots_all = expert_count * capacity
    w_gate = gate_weight[0, 0]
    w_up = up_weight[0, 0]
    w_down = down_weight[0, 0]
    w_router = router_weight[0]
    picks = routes[0]

    experts = jnp.arange(expert_count, dtype=jnp.int32)
    hit = picks[:, :, None] == experts[None, None, :]
    per_token = jnp.sum(hit.astype(jnp.float32), axis=1).astype(jnp.bfloat16)
    token_ids = jnp.arange(token_count, dtype=jnp.int32)
    before = (token_ids[None, :] < token_ids[:, None]).astype(jnp.bfloat16)
    earlier = jnp.dot(before, per_token, preferred_element_type=jnp.float32).astype(jnp.int32)
    rank_inside = jnp.sum(jnp.where(hit, earlier[:, None, :], 0), axis=2)
    slot_index = jnp.where(picks < expert_count, picks * capacity + rank_inside, slots_all)

    exponent = jnp.exp(route_logits[0])
    route_weight = exponent / jnp.sum(exponent, axis=1, keepdims=True)

    slot_ids = jnp.arange(slots_all, dtype=jnp.int32).reshape(expert_count, capacity)
    pack = jnp.zeros((expert_count, capacity, token_count), jnp.float32)
    combine = jnp.zeros((token_count, expert_count, capacity), jnp.float32)
    for k in range(top_count):
        chosen = slot_index[:, k]
        pack = pack + (slot_ids[:, :, None] == chosen[None, None, :]).astype(jnp.float32)
        combine = combine + jnp.where(
            chosen[:, None, None] == slot_ids[None, :, :], route_weight[:, k][:, None, None], 0.0
        )
    pack = pack.astype(jnp.bfloat16)
    combine_bf16 = combine.astype(jnp.bfloat16)
    pack, combine_bf16 = lax.optimization_barrier((pack, combine_bf16))

    def pack_rows(rows):
        sent = jnp.einsum("est,td->esd", pack, rows, preferred_element_type=jnp.float32)
        return sent.astype(jnp.bfloat16)

    def exchange(block):
        return lax.all_to_all(block, "expert", split_axis=0, concat_axis=0, tiled=True)

    sent = jnp.concatenate([pack_rows(x_in), jnp.zeros_like(pack_rows(x_in))], axis=2)
    sent = lax.optimization_barrier(sent)
    got = exchange(lax.dynamic_update_slice(sent, pack_rows(incoming), (0, 0, width_model)))
    inputs = got[:, :, :width_model]
    grad_rows = got[:, :, width_model:]
    lanes = 128
    wide = width_model + lanes
    pad_cols = jnp.zeros((lanes, w_gate.shape[1]), w_gate.dtype)
    w_gate_wide = jnp.concatenate([w_gate, pad_cols], axis=0)
    w_up_wide = jnp.concatenate([w_up, pad_cols], axis=0)
    hidden_count = w_gate.shape[1]
    pre_both = jnp.einsum(
        "esd,df->esf", inputs, jnp.concatenate([w_gate, w_up], axis=1),
        preferred_element_type=jnp.float32,
    )
    pre_gate = pre_both[:, :, :hidden_count]
    pre_up = pre_both[:, :, hidden_count:]
    hidden_grad = jnp.einsum("esd,fd->esf", grad_rows, w_down, preferred_element_type=jnp.float32)
    sigmoid_gate = jax.nn.sigmoid(pre_gate)
    activation = pre_gate * sigmoid_gate
    pair_dots = jnp.sum(hidden_grad * activation * pre_up, axis=-1).astype(jnp.bfloat16)
    gate_grad = (
        hidden_grad * pre_up * sigmoid_gate * (1.0 + pre_gate * (1.0 - sigmoid_gate))
    ).astype(jnp.bfloat16)
    up_grad = (hidden_grad * activation).astype(jnp.bfloat16)
    pair_rows = jnp.einsum(
        "esf,df->esd", gate_grad, w_gate_wide, preferred_element_type=jnp.float32
    ) + jnp.einsum("esf,df->esd", up_grad, w_up_wide, preferred_element_type=jnp.float32)
    lane_ids = jnp.arange(wide, dtype=jnp.int32)[None, None, :]
    pair_rows = jnp.where(
        lane_ids == width_model, pair_dots.astype(jnp.float32)[:, :, None], pair_rows
    )
    returned = exchange(pair_rows.astype(jnp.bfloat16))
    returned_dots = returned[:, :, width_model]

    slot_dots = returned_dots.astype(jnp.float32)
    weight_grad = jnp.sum(
        jnp.where(
            slot_index[:, :, None, None] == slot_ids[None, None, :, :],
            slot_dots[None, None, :, :],
            0.0,
        ),
        axis=(2, 3),
    )
    center = jnp.sum(route_weight * weight_grad, axis=1, keepdims=True)
    logit_grad = route_weight * (weight_grad - center)
    matches = picks[:, :, None] == jnp.arange(every_expert, dtype=jnp.int32)[None, None, :]
    dense_grad = jnp.sum(jnp.where(matches, logit_grad[:, :, None], 0.0), axis=1)
    router_grad = jnp.zeros((token_count, width_model), jnp.float32)
    for part in split_bf16(dense_grad, 3):
        router_grad = router_grad + lax.dot_general(
            part, w_router, (((1,), (1,)), ((), ())), preferred_element_type=jnp.float32
        )
    expert_sum = jnp.einsum(
        "tes,esd->td", combine_bf16, returned, preferred_element_type=jnp.float32
    )[:, :width_model]
    grad_in = (incoming.astype(jnp.float32) + expert_sum + router_grad).astype(jnp.bfloat16)
    return (grad_in[None], logit_grad[None])


def solution(mesh):
    in_specs = (
        P("section", "expert", None),
        P("section", "expert", None),
        P("section", "expert", None),
        P("section", "expert", None),
        P("section", "expert", None, None),
        P("section", "expert", None, None),
        P("section", "expert", None, None),
        P("section", None, None),
    )
    out_specs = (P("section", "expert", None), P("section", "expert", None))
    return jax.shard_map(
        per_device, mesh=mesh, in_specs=in_specs, out_specs=out_specs, check_vma=False
    )
```

```python
import jax
import jax.numpy as jnp
from jax import lax
from jax.sharding import PartitionSpec as P


def from_behind(shard, axis, by):
    size = lax.axis_size(axis)
    return lax.ppermute(shard, axis, [(i, (i + by) % size) for i in range(size)])


def split_bf16(values, parts):
    pieces = []
    rest = values
    for _ in range(parts):
        piece = rest.astype(jnp.bfloat16)
        pieces.append(piece)
        rest = rest - piece.astype(jnp.float32)
    return pieces


def per_device(
    grad_out, layer_input, routes, route_logits, gate_weight, up_weight, down_weight, router_weight
):
    incoming = from_behind(grad_out, "section", -1)[0]
    x_in = layer_input[0]
    token_count, width_model = x_in.shape
    top_count = routes.shape[2]
    expert_count = lax.axis_size("expert")
    every_expert = router_weight.shape[2]
    capacity = 2 * token_count * top_count // every_expert
    slots_all = expert_count * capacity
    w_gate = gate_weight[0, 0]
    w_up = up_weight[0, 0]
    w_down = down_weight[0, 0]
    w_router = router_weight[0]
    picks = routes[0]

    experts = jnp.arange(expert_count, dtype=jnp.int32)
    hit = picks[:, :, None] == experts[None, None, :]
    per_token = jnp.sum(hit.astype(jnp.float32), axis=1).astype(jnp.bfloat16)
    token_ids = jnp.arange(token_count, dtype=jnp.int32)
    before = (token_ids[None, :] < token_ids[:, None]).astype(jnp.bfloat16)
    earlier = jnp.dot(before, per_token, preferred_element_type=jnp.float32).astype(jnp.int32)
    rank_inside = jnp.sum(jnp.where(hit, earlier[:, None, :], 0), axis=2)
    slot_index = jnp.where(picks < expert_count, picks * capacity + rank_inside, slots_all)

    exponent = jnp.exp(route_logits[0])
    route_weight = exponent / jnp.sum(exponent, axis=1, keepdims=True)

    slot_ids = jnp.arange(slots_all, dtype=jnp.int32).reshape(expert_count, capacity)
    pack = jnp.zeros((expert_count, capacity, token_count), jnp.float32)
    combine = jnp.zeros((token_count, expert_count, capacity), jnp.float32)
    for k in range(top_count):
        chosen = slot_index[:, k]
        pack = pack + (slot_ids[:, :, None] == chosen[None, None, :]).astype(jnp.float32)
        combine = combine + jnp.where(
            chosen[:, None, None] == slot_ids[None, :, :], route_weight[:, k][:, None, None], 0.0
        )
    pack = pack.astype(jnp.bfloat16)
    combine_parts = jnp.stack(split_bf16(combine, 2))
    pack, combine_parts = lax.optimization_barrier((pack, combine_parts))

    def pack_rows(rows):
        sent = jnp.einsum("est,td->esd", pack, rows, preferred_element_type=jnp.float32)
        return sent.astype(jnp.bfloat16)

    def exchange(block):
        return lax.all_to_all(block, "expert", split_axis=0, concat_axis=0, tiled=True)

    sent = jnp.concatenate([pack_rows(x_in), jnp.zeros_like(pack_rows(x_in))], axis=2)
    sent = lax.optimization_barrier(sent)
    got = exchange(lax.dynamic_update_slice(sent, pack_rows(incoming), (0, 0, width_model)))
    inputs = got[:, :, :width_model]
    grad_rows = got[:, :, width_model:]
    lanes = 128
    wide = width_model + lanes
    pad_cols = jnp.zeros((lanes, w_gate.shape[1]), w_gate.dtype)
    w_gate_wide = jnp.concatenate([w_gate, pad_cols], axis=0)
    w_up_wide = jnp.concatenate([w_up, pad_cols], axis=0)
    hidden_count = w_gate.shape[1]
    pre_both = jnp.einsum(
        "esd,df->esf", inputs, jnp.concatenate([w_gate, w_up], axis=1),
        preferred_element_type=jnp.float32,
    )
    pre_gate = pre_both[:, :, :hidden_count]
    pre_up = pre_both[:, :, hidden_count:]
    hidden_grad = jnp.einsum("esd,fd->esf", grad_rows, w_down, preferred_element_type=jnp.float32)
    sigmoid_gate = jax.nn.sigmoid(pre_gate)
    activation = pre_gate * sigmoid_gate
    pair_dots = jnp.sum(hidden_grad * activation * pre_up, axis=-1).astype(jnp.bfloat16)
    gate_grad = (
        hidden_grad * pre_up * sigmoid_gate * (1.0 + pre_gate * (1.0 - sigmoid_gate))
    ).astype(jnp.bfloat16)
    up_grad = (hidden_grad * activation).astype(jnp.bfloat16)
    pair_rows = jnp.einsum(
        "esf,df->esd", gate_grad, w_gate_wide, preferred_element_type=jnp.float32
    ) + jnp.einsum("esf,df->esd", up_grad, w_up_wide, preferred_element_type=jnp.float32)
    own_column = lax.dynamic_index_in_dim(w_router, lax.axis_index("expert"), 1, False)
    own_column = jnp.concatenate(
        [own_column.astype(jnp.float32), jnp.zeros((lanes,), jnp.float32)]
    )
    pair_rows = pair_rows + pair_dots.astype(jnp.float32)[:, :, None] * own_column[None, None, :]
    lane_ids = jnp.arange(wide, dtype=jnp.int32)[None, None, :]
    pair_rows = jnp.where(
        lane_ids == width_model, pair_dots.astype(jnp.float32)[:, :, None], pair_rows
    )
    returned = exchange(pair_rows.astype(jnp.bfloat16))
    returned_dots = returned[:, :, width_model]

    slot_dots = returned_dots.astype(jnp.float32)
    weight_grad = jnp.sum(
        jnp.where(
            slot_index[:, :, None, None] == slot_ids[None, None, :, :],
            slot_dots[None, None, :, :],
            0.0,
        ),
        axis=(2, 3),
    )
    center = jnp.sum(route_weight * weight_grad, axis=1, keepdims=True)
    logit_grad = route_weight * (weight_grad - center)
    matches = picks[:, :, None] == jnp.arange(every_expert, dtype=jnp.int32)[None, None, :]
    dense_weight = jnp.sum(jnp.where(matches, route_weight[:, :, None], 0.0), axis=1)
    mean_column = jnp.zeros((token_count, width_model), jnp.float32)
    for part in split_bf16(dense_weight, 3):
        mean_column = mean_column + lax.dot_general(
            part, w_router, (((1,), (1,)), ((), ())), preferred_element_type=jnp.float32
        )
    expert_both = jnp.einsum(
        "ptes,esd->ptd", combine_parts, returned, preferred_element_type=jnp.float32
    )
    expert_sum = expert_both[0, :, :width_model] + expert_both[1, :, :width_model]
    router_rest = -center * mean_column
    grad_in = (incoming.astype(jnp.float32) + expert_sum + router_rest).astype(jnp.bfloat16)
    return (grad_in[None], logit_grad[None])


def solution(mesh):
    in_specs = (
        P("section", "expert", None),
        P("section", "expert", None),
        P("section", "expert", None),
        P("section", "expert", None),
        P("section", "expert", None, None),
        P("section", "expert", None, None),
        P("section", "expert", None, None),
        P("section", None, None),
    )
    out_specs = (P("section", "expert", None), P("section", "expert", None))
    return jax.shard_map(
        per_device, mesh=mesh, in_specs=in_specs, out_specs=out_specs, check_vma=False
    )
```

```python
import jax
import jax.numpy as jnp
from jax import lax
from jax.sharding import PartitionSpec as P


def from_behind(shard, axis, by):
    size = lax.axis_size(axis)
    return lax.ppermute(shard, axis, [(i, (i + by) % size) for i in range(size)])


def split_bf16(values, parts):
    pieces = []
    rest = values
    for _ in range(parts):
        piece = rest.astype(jnp.bfloat16)
        pieces.append(piece)
        rest = rest - piece.astype(jnp.float32)
    return pieces


def per_device(
    grad_out, layer_input, routes, route_logits, gate_weight, up_weight, down_weight, router_weight
):
    incoming = from_behind(grad_out, "section", -1)[0]
    x_in = layer_input[0]
    token_count, width_model = x_in.shape
    top_count = routes.shape[2]
    expert_count = lax.axis_size("expert")
    every_expert = router_weight.shape[2]
    capacity = 2 * token_count * top_count // every_expert
    slots_all = expert_count * capacity
    w_gate = gate_weight[0, 0]
    w_up = up_weight[0, 0]
    w_down = down_weight[0, 0]
    w_router = router_weight[0]
    picks = routes[0]

    experts = jnp.arange(expert_count, dtype=jnp.int32)
    hit = picks[:, :, None] == experts[None, None, :]
    per_token = jnp.sum(hit.astype(jnp.float32), axis=1).astype(jnp.bfloat16)
    token_ids = jnp.arange(token_count, dtype=jnp.int32)
    before = (token_ids[None, :] < token_ids[:, None]).astype(jnp.bfloat16)
    earlier = jnp.dot(before, per_token, preferred_element_type=jnp.float32).astype(jnp.int32)
    rank_inside = jnp.sum(jnp.where(hit, earlier[:, None, :], 0), axis=2)
    slot_index = jnp.where(picks < expert_count, picks * capacity + rank_inside, slots_all)

    exponent = jnp.exp(route_logits[0])
    route_weight = exponent / jnp.sum(exponent, axis=1, keepdims=True)

    slot_ids = jnp.arange(slots_all, dtype=jnp.int32).reshape(expert_count, capacity)
    pack = jnp.zeros((expert_count, capacity, token_count), jnp.float32)
    combine = jnp.zeros((token_count, expert_count, capacity), jnp.float32)
    for k in range(top_count):
        chosen = slot_index[:, k]
        pack = pack + (slot_ids[:, :, None] == chosen[None, None, :]).astype(jnp.float32)
        combine = combine + jnp.where(
            chosen[:, None, None] == slot_ids[None, :, :], route_weight[:, k][:, None, None], 0.0
        )
    pack = pack.astype(jnp.bfloat16)
    combine_bf16 = combine.astype(jnp.bfloat16)
    pack, combine_bf16 = lax.optimization_barrier((pack, combine_bf16))

    def pack_rows(rows):
        sent = jnp.einsum("est,td->esd", pack, rows, preferred_element_type=jnp.float32)
        return sent.astype(jnp.bfloat16)

    def exchange(block):
        return lax.all_to_all(block, "expert", split_axis=0, concat_axis=0, tiled=True)

    sent = jnp.concatenate([pack_rows(x_in), jnp.zeros_like(pack_rows(x_in))], axis=2)
    sent = lax.optimization_barrier(sent)
    got = exchange(lax.dynamic_update_slice(sent, pack_rows(incoming), (0, 0, width_model)))
    inputs = got[:, :, :width_model]
    grad_rows = got[:, :, width_model:]
    lanes = 128
    wide = width_model + lanes
    pad_cols = jnp.zeros((lanes, w_gate.shape[1]), w_gate.dtype)
    w_gate_wide = jnp.concatenate([w_gate, pad_cols], axis=0)
    w_up_wide = jnp.concatenate([w_up, pad_cols], axis=0)
    hidden_count = w_gate.shape[1]
    pre_both = jnp.einsum(
        "esd,df->esf", inputs, jnp.concatenate([w_gate, w_up], axis=1),
        preferred_element_type=jnp.float32,
    )
    pre_gate = pre_both[:, :, :hidden_count]
    pre_up = pre_both[:, :, hidden_count:]
    hidden_grad = jnp.einsum("esd,fd->esf", grad_rows, w_down, preferred_element_type=jnp.float32)
    sigmoid_gate = jax.nn.sigmoid(pre_gate)
    activation = pre_gate * sigmoid_gate
    pair_dots = jnp.sum(hidden_grad * activation * pre_up, axis=-1).astype(jnp.bfloat16)
    gate_grad = (
        hidden_grad * pre_up * sigmoid_gate * (1.0 + pre_gate * (1.0 - sigmoid_gate))
    ).astype(jnp.bfloat16)
    up_grad = (hidden_grad * activation).astype(jnp.bfloat16)
    pair_rows = jnp.einsum(
        "esf,df->esd", gate_grad, w_gate_wide, preferred_element_type=jnp.float32
    ) + jnp.einsum("esf,df->esd", up_grad, w_up_wide, preferred_element_type=jnp.float32)
    own_column = lax.dynamic_index_in_dim(w_router, lax.axis_index("expert"), 1, False)
    own_column = jnp.concatenate(
        [own_column.astype(jnp.float32), jnp.zeros((lanes,), jnp.float32)]
    )
    pair_rows = pair_rows + pair_dots.astype(jnp.float32)[:, :, None] * own_column[None, None, :]
    lane_ids = jnp.arange(wide, dtype=jnp.int32)[None, None, :]
    pair_rows = jnp.where(
        lane_ids == width_model, pair_dots.astype(jnp.float32)[:, :, None], pair_rows
    )
    returned = exchange(pair_rows.astype(jnp.bfloat16))
    returned_dots = returned[:, :, width_model]

    slot_dots = returned_dots.astype(jnp.float32)
    weight_grad = jnp.sum(
        jnp.where(
            slot_index[:, :, None, None] == slot_ids[None, None, :, :],
            slot_dots[None, None, :, :],
            0.0,
        ),
        axis=(2, 3),
    )
    center = jnp.sum(route_weight * weight_grad, axis=1, keepdims=True)
    logit_grad = route_weight * (weight_grad - center)
    matches = picks[:, :, None] == jnp.arange(every_expert, dtype=jnp.int32)[None, None, :]
    dense_weight = jnp.sum(jnp.where(matches, route_weight[:, :, None], 0.0), axis=1)
    mean_column = jnp.zeros((token_count, width_model), jnp.float32)
    for part in split_bf16(dense_weight, 3):
        mean_column = mean_column + lax.dot_general(
            part, w_router, (((1,), (1,)), ((), ())), preferred_element_type=jnp.float32
        )
    expert_sum = jnp.einsum(
        "tes,esd->td", combine_bf16, returned, preferred_element_type=jnp.float32
    )[:, :width_model]
    router_rest = -center * mean_column
    grad_in = (incoming.astype(jnp.float32) + expert_sum + router_rest).astype(jnp.bfloat16)
    return (grad_in[None], logit_grad[None])


def solution(mesh):
    in_specs = (
        P("section", "expert", None),
        P("section", "expert", None),
        P("section", "expert", None),
        P("section", "expert", None),
        P("section", "expert", None, None),
        P("section", "expert", None, None),
        P("section", "expert", None, None),
        P("section", None, None),
    )
    out_specs = (P("section", "expert", None), P("section", "expert", None))
    return jax.shard_map(
        per_device, mesh=mesh, in_specs=in_specs, out_specs=out_specs, check_vma=False
    )
```

```python
import jax
import jax.numpy as jnp
from jax import lax
from jax.sharding import PartitionSpec as P


def from_behind(shard, axis, by):
    size = lax.axis_size(axis)
    return lax.ppermute(shard, axis, [(i, (i + by) % size) for i in range(size)])


def split_bf16(values, parts):
    pieces = []
    rest = values
    for _ in range(parts):
        piece = rest.astype(jnp.bfloat16)
        pieces.append(piece)
        rest = rest - piece.astype(jnp.float32)
    return pieces


def per_device(
    grad_out, layer_input, routes, route_logits, gate_weight, up_weight, down_weight, router_weight
):
    incoming = from_behind(grad_out, "section", -1)[0]
    x_in = layer_input[0]
    token_count, width_model = x_in.shape
    top_count = routes.shape[2]
    expert_count = lax.axis_size("expert")
    every_expert = router_weight.shape[2]
    capacity = 2 * token_count * top_count // every_expert
    slots_all = expert_count * capacity
    w_gate = gate_weight[0, 0]
    w_up = up_weight[0, 0]
    w_down = down_weight[0, 0]
    w_router = router_weight[0]
    picks = routes[0]

    experts = jnp.arange(expert_count, dtype=jnp.int32)
    hit = picks[:, :, None] == experts[None, None, :]
    per_token = jnp.sum(hit.astype(jnp.float32), axis=1).astype(jnp.bfloat16)
    token_ids = jnp.arange(token_count, dtype=jnp.int32)
    before = (token_ids[None, :] < token_ids[:, None]).astype(jnp.bfloat16)
    earlier = jnp.dot(before, per_token, preferred_element_type=jnp.float32).astype(jnp.int32)
    rank_inside = jnp.sum(jnp.where(hit, earlier[:, None, :], 0), axis=2)
    slot_index = jnp.where(picks < expert_count, picks * capacity + rank_inside, slots_all)

    exponent = jnp.exp(route_logits[0])
    route_weight = exponent / jnp.sum(exponent, axis=1, keepdims=True)

    slot_ids = jnp.arange(slots_all, dtype=jnp.int32).reshape(expert_count, capacity)
    pack = jnp.zeros((expert_count, capacity, token_count), jnp.float32)
    combine = jnp.zeros((token_count, expert_count, capacity), jnp.float32)
    for k in range(top_count):
        chosen = slot_index[:, k]
        pack = pack + (slot_ids[:, :, None] == chosen[None, None, :]).astype(jnp.float32)
        combine = combine + jnp.where(
            chosen[:, None, None] == slot_ids[None, :, :], route_weight[:, k][:, None, None], 0.0
        )
    pack = pack.astype(jnp.bfloat16)
    combine_bf16 = combine.astype(jnp.bfloat16)
    pick_slot = (
        slot_index.reshape(-1)[:, None, None] == slot_ids[None, :, :]
    ).astype(jnp.bfloat16)
    pack, combine_bf16, pick_slot = lax.optimization_barrier((pack, combine_bf16, pick_slot))

    def pack_rows(rows):
        sent = jnp.einsum("est,td->esd", pack, rows, preferred_element_type=jnp.float32)
        return sent.astype(jnp.bfloat16)

    def exchange(block):
        return lax.all_to_all(block, "expert", split_axis=0, concat_axis=0, tiled=True)

    sent = jnp.concatenate([pack_rows(x_in), jnp.zeros_like(pack_rows(x_in))], axis=2)
    sent = lax.optimization_barrier(sent)
    got = exchange(lax.dynamic_update_slice(sent, pack_rows(incoming), (0, 0, width_model)))
    inputs = got[:, :, :width_model]
    grad_rows = got[:, :, width_model:]
    lanes = 128
    wide = width_model + lanes
    pad_cols = jnp.zeros((lanes, w_gate.shape[1]), w_gate.dtype)
    w_gate_wide = jnp.concatenate([w_gate, pad_cols], axis=0)
    w_up_wide = jnp.concatenate([w_up, pad_cols], axis=0)
    hidden_count = w_gate.shape[1]
    pre_both = jnp.einsum(
        "esd,df->esf", inputs, jnp.concatenate([w_gate, w_up], axis=1),
        preferred_element_type=jnp.float32,
    )
    pre_gate = pre_both[:, :, :hidden_count]
    pre_up = pre_both[:, :, hidden_count:]
    hidden_grad = jnp.einsum("esd,fd->esf", grad_rows, w_down, preferred_element_type=jnp.float32)
    sigmoid_gate = jax.nn.sigmoid(pre_gate)
    activation = pre_gate * sigmoid_gate
    pair_dots = jnp.sum(hidden_grad * activation * pre_up, axis=-1).astype(jnp.bfloat16)
    gate_grad = (
        hidden_grad * pre_up * sigmoid_gate * (1.0 + pre_gate * (1.0 - sigmoid_gate))
    ).astype(jnp.bfloat16)
    up_grad = (hidden_grad * activation).astype(jnp.bfloat16)
    pair_rows = jnp.einsum(
        "esf,df->esd", gate_grad, w_gate_wide, preferred_element_type=jnp.float32
    ) + jnp.einsum("esf,df->esd", up_grad, w_up_wide, preferred_element_type=jnp.float32)
    own_column = lax.dynamic_index_in_dim(w_router, lax.axis_index("expert"), 1, False)
    own_column = jnp.concatenate(
        [own_column.astype(jnp.float32), jnp.zeros((lanes,), jnp.float32)]
    )
    pair_rows = pair_rows + pair_dots.astype(jnp.float32)[:, :, None] * own_column[None, None, :]
    lane_ids = jnp.arange(wide, dtype=jnp.int32)[None, None, :]
    pair_rows = jnp.where(
        lane_ids == width_model, pair_dots.astype(jnp.float32)[:, :, None], pair_rows
    )
    returned = exchange(pair_rows.astype(jnp.bfloat16))
    weight_grad = jnp.einsum(
        "pes,esl->pl", pick_slot, returned[:, :, width_model:], preferred_element_type=jnp.float32
    )[:, 0].reshape(token_count, top_count)
    center = jnp.sum(route_weight * weight_grad, axis=1, keepdims=True)
    logit_grad = route_weight * (weight_grad - center)
    matches = picks[:, :, None] == jnp.arange(every_expert, dtype=jnp.int32)[None, None, :]
    dense_weight = jnp.sum(jnp.where(matches, route_weight[:, :, None], 0.0), axis=1)
    mean_column = jnp.zeros((token_count, width_model), jnp.float32)
    for part in split_bf16(dense_weight, 3):
        mean_column = mean_column + lax.dot_general(
            part, w_router, (((1,), (1,)), ((), ())), preferred_element_type=jnp.float32
        )
    expert_sum = jnp.einsum(
        "tes,esd->td", combine_bf16, returned, preferred_element_type=jnp.float32
    )[:, :width_model]
    router_rest = -center * mean_column
    grad_in = (incoming.astype(jnp.float32) + expert_sum + router_rest).astype(jnp.bfloat16)
    return (grad_in[None], logit_grad[None])


def solution(mesh):
    in_specs = (
        P("section", "expert", None),
        P("section", "expert", None),
        P("section", "expert", None),
        P("section", "expert", None),
        P("section", "expert", None, None),
        P("section", "expert", None, None),
        P("section", "expert", None, None),
        P("section", None, None),
    )
    out_specs = (P("section", "expert", None), P("section", "expert", None))
    return jax.shard_map(
        per_device, mesh=mesh, in_specs=in_specs, out_specs=out_specs, check_vma=False
    )
```
